512 devices in a mesh: group: 8 (over z_lo, core), dp: 8 (over y), tensor: 8 (over z_hi, x).
Axes of the slice: x: 4, y: 8, z: 8 (z_hi: 2, z_lo: 4; z = z_hi * 4 + z_lo), core: 2. Of those that a mesh axis runs over, the one named last changes fastest.
Arguments:
- keyvalue_local: float32 [8, 2, 4096, 1024], P('group', None, 'dp', 'tensor'), may hold values from -6 to 6
- keyvalue_anchor: float32 [2, 4096, 1024], P(None, 'dp', 'tensor'), may hold values from -6 to 6
- keyvalue_state: float32 [2, 4096, 1024], P(None, 'dp', 'tensor'), may hold values from -6 to 6
- router_local: float32 [8, 4096, 8], P('group', 'dp'), may hold values from -6 to 6
- router_anchor: float32 [4096, 8], P('dp'), may hold values from -6 to 6
- router_state: float32 [4096, 8], P('dp'), may hold values from -6 to 6
- gain_local: float32 [8, 2, 4096], P('group', None, 'dp'), may hold values from -6 to 6
- gain_anchor: float32 [2, 4096], P(None, 'dp'), may hold values from -6 to 6
- gain_state: float32 [2, 4096], P(None, 'dp'), may hold values from -6 to 6
- embed_local: float32 [8, 1000, 4096], P('group', 'dp', 'tensor'), may hold values from -6 to 6
- embed_anchor: float32 [1000, 4096], P('dp', 'tensor'), may hold values from -6 to 6
- embed_state: float32 [1000, 4096], P('dp', 'tensor'), may hold values from -6 to 6
- embed_basis: float32 [4096, 64], P('tensor'), may hold values from -0.25 to 0.25
- outer_rate: float32 [], replicated, may hold values from 0.5 to 1
Outputs:
- keyvalue_average: float32 [2, 4096, 1024], P(None, 'dp', 'tensor')
- keyvalue_momentum: float32 [2, 4096, 1024], P(None, 'dp', 'tensor')
- keyvalue_updated: float32 [2, 4096, 1024], P(None, 'dp', 'tensor')
- router_average: float32 [4096, 8], P('dp')
- router_momentum: float32 [4096, 8], P('dp')
- router_updated: float32 [4096, 8], P('dp')
- gain_average: float32 [2, 4096], P(None, 'dp')
- gain_momentum: float32 [2, 4096], P(None, 'dp')
- gain_updated: float32 [2, 4096], P(None, 'dp')
- embed_average: float32 [1000, 4096], P('dp', 'tensor')
- embed_momentum: float32 [1000, 4096], P('dp', 'tensor')
- embed_updated: float32 [1000, 4096], P('dp', 'tensor')
The draws below stay inside these ranges and needn't reach their ends.
All inputs are finite; a program needn't handle non-finite values.
Results may differ from the reference program's by a relative error of at most 0.0001.
Values sent between devices are 32-bit elements; how exact they have to be, the bound alone decides.
No kernel may reach another device: no remote copies, remote signals or barrier semaphores. Data moves between devices by JAX's collectives and lax.ppermute only.
A program may use at most 64 MiB of HBM per device.

```python
import math
import jax
import jax.numpy as jnp
from jax import lax

D = 4096
KV = 1024
EXPERTS = 8
RANK = 64
VOCAB = 1000
GROUPS = 8


def level_of(own_key, shape, shards, least, high):
    def one(axis_at, blocks):
        heights = jax.random.uniform(jax.random.fold_in(jax.random.fold_in(own_key, 6), axis_at), (blocks,), jnp.float32, least / len(shards), high / len(shards))
        return jnp.repeat(jnp.exp(heights), shape[axis_at] // blocks).reshape((-1,) + (1,) * (len(shape) - axis_at - 1))

    gain = one(*shards[0])
    for cut in shards[1:]:
        gain = gain * one(*cut)
    return gain


def centred(rng, shape, spread, bound, pieces=(), held_as=jnp.bfloat16):
    values = spread * jax.random.normal(rng, shape, jnp.float32)
    if pieces:
        values = values * level_of(rng, shape, pieces, -0.22, 0.18)
    return jnp.clip(values, -bound, bound).astype(held_as)


def setup_inputs(seed: int = 0) -> dict:
    seeds = jax.random.split(jax.random.key(seed), 15)
    keyvalue_local = centred(seeds[0], (GROUPS, 2, D, KV), 1.0, 6.0, ((0, 8), (2, 8), (3, 8)), jnp.float32)
    keyvalue_anchor = centred(seeds[1], (2, D, KV), 1.0, 6.0, ((1, 8), (2, 8)), jnp.float32)
    keyvalue_state = centred(seeds[2], (2, D, KV), 1.0, 6.0, ((1, 8), (2, 8)), jnp.float32)
    router_local = centred(seeds[3], (GROUPS, D, EXPERTS), 1.0, 6.0, ((0, 8), (1, 8)), jnp.float32)
    router_anchor = centred(seeds[4], (D, EXPERTS), 1.0, 6.0, ((0, 8),), jnp.float32)
    router_state = centred(seeds[5], (D, EXPERTS), 1.0, 6.0, ((0, 8),), jnp.float32)
    gain_local = centred(seeds[6], (GROUPS, 2, D), 1.0, 6.0, ((0, 8), (2, 8)), jnp.float32)
    gain_anchor = centred(seeds[7], (2, D), 1.0, 6.0, ((1, 8),), jnp.float32)
    gain_state = centred(seeds[8], (2, D), 1.0, 6.0, ((1, 8),), jnp.float32)
    embed_local = centred(seeds[9], (GROUPS, VOCAB, D), 1.0, 6.0, ((0, 8), (1, 8), (2, 8)), jnp.float32)
    embed_anchor = centred(seeds[10], (VOCAB, D), 1.0, 6.0, ((0, 8), (1, 8)), jnp.float32)
    embed_state = centred(seeds[11], (VOCAB, D), 1.0, 6.0, ((0, 8), (1, 8)), jnp.float32)
    embed_basis = centred(seeds[12], (D, RANK), (D // 8) ** -0.5, 0.25, ((0, 8),), jnp.float32)
    outer_rate = jnp.clip(jnp.exp(jax.random.uniform(seeds[13], (), jnp.float32, math.log(0.5), math.log(1.0))), 0.5, 1.0)
    return dict(keyvalue_local=keyvalue_local, keyvalue_anchor=keyvalue_anchor, keyvalue_state=keyvalue_state, router_local=router_local, router_anchor=router_anchor, router_state=router_state, gain_local=gain_local, gain_anchor=gain_anchor, gain_state=gain_state, embed_local=embed_local, embed_anchor=embed_anchor, embed_state=embed_state, embed_basis=embed_basis, outer_rate=outer_rate)


def nesterov(average, state, anchor, outer_rate):
    momentum = 0.5 * state + average
    updated = anchor - outer_rate * (average + 0.5 * momentum)
    return average, momentum, updated


def group_mean(anchor, local):
    total = jnp.zeros(anchor.shape, jnp.float32)
    for index in range(GROUPS):
        total = total + (anchor - local[index])
    return total / GROUPS


def reference(keyvalue_local, keyvalue_anchor, keyvalue_state, router_local, router_anchor, router_state, gain_local, gain_anchor, gain_state, embed_local, embed_anchor, embed_state, embed_basis, outer_rate):
    keyvalue_out = nesterov(group_mean(keyvalue_anchor, keyvalue_local), keyvalue_state, keyvalue_anchor, outer_rate)
    router_out = nesterov(group_mean(router_anchor, router_local), router_state, router_anchor, outer_rate)
    gain_out = nesterov(group_mean(gain_anchor, gain_local), gain_state, gain_anchor, outer_rate)
    factors = jnp.zeros((embed_anchor.shape[0], embed_basis.shape[1]), jnp.float32)
    for index in range(GROUPS):
        factors = factors + jnp.dot(embed_anchor - embed_local[index], embed_basis, precision=lax.Precision.HIGHEST, preferred_element_type=jnp.float32)
    factors = factors / GROUPS
    embed_average = jnp.dot(factors, embed_basis.T, precision=lax.Precision.HIGHEST, preferred_element_type=jnp.float32)
    embed_out = nesterov(embed_average, embed_state, embed_anchor, outer_rate)
    return (keyvalue_out[0], keyvalue_out[1], keyvalue_out[2], router_out[0], router_out[1], router_out[2], gain_out[0], gain_out[1], gain_out[2], embed_out[0], embed_out[1], embed_out[2])
```

```python
import jax
import jax.numpy as jnp
from jax import lax
from jax.sharding import PartitionSpec as P

HIGHEST = lax.Precision.HIGHEST
MODE = "separate"


def nesterov(average, state, anchor, outer_rate):
    momentum = 0.5 * state + average
    updated = anchor - outer_rate * (average + 0.5 * momentum)
    return (average, momentum, updated)


def local(kv_local, kv_anchor, kv_state, r_local, r_anchor, r_state, g_local, g_anchor, g_state,
          e_local, e_anchor, e_state, basis, rate):
    groups = lax.axis_size("group")
    kv_diff = kv_anchor - kv_local[0]
    r_diff = r_anchor - r_local[0]
    g_diff = g_anchor - g_local[0]
    partial = jnp.dot(e_anchor - e_local[0], basis, precision=HIGHEST, preferred_element_type=jnp.float32)
    if MODE == "concat":
        partial = lax.psum(partial, "tensor")
        pieces = (kv_diff, r_diff, g_diff, partial)
        flat = jnp.concatenate([p.reshape(-1) for p in pieces])
        total = lax.psum(flat, "group")
        sums, at = [], 0
        for p in pieces:
            sums.append(total[at:at + p.size].reshape(p.shape))
            at += p.size
        kv_sum, r_sum, g_sum, factors = sums
    elif MODE == "separate":
        partial = lax.psum(partial, "tensor")
        kv_sum, r_sum, g_sum, factors = lax.psum((kv_diff, r_diff, g_diff, partial), "group")
    elif MODE == "nested":
        kv_sum, r_sum, g_sum = lax.psum((kv_diff, r_diff, g_diff), "group")
        factors = lax.psum(lax.psum(partial, "tensor"), "group")
    kv_out = nesterov(kv_sum / groups, kv_state, kv_anchor, rate)
    r_out = nesterov(r_sum / groups, r_state, r_anchor, rate)
    g_out = nesterov(g_sum / groups, g_state, g_anchor, rate)
    factors = factors / groups
    e_avg = jnp.dot(factors, basis.T, precision=HIGHEST, preferred_element_type=jnp.float32)
    e_out = nesterov(e_avg, e_state, e_anchor, rate)
    return (*kv_out, *r_out, *g_out, *e_out)


IN_SPECS = (
    P("group", None, "dp", "tensor"), P(None, "dp", "tensor"), P(None, "dp", "tensor"),
    P("group", "dp", None), P("dp", None), P("dp", None),
    P("group", None, "dp"), P(None, "dp"), P(None, "dp"),
    P("group", "dp", "tensor"), P("dp", "tensor"), P("dp", "tensor"),
    P("tensor", None), P(),
)
OUT_SPECS = (
    P(None, "dp", "tensor"), P(None, "dp", "tensor"), P(None, "dp", "tensor"),
    P("dp", None), P("dp", None), P("dp", None),
    P(None, "dp"), P(None, "dp"), P(None, "dp"),
    P("dp", "tensor"), P("dp", "tensor"), P("dp", "tensor"),
)


def solution(mesh):
    return jax.shard_map(local, mesh=mesh, in_specs=IN_SPECS, out_specs=OUT_SPECS, check_vma=False)
```

```python
import jax
import jax.numpy as jnp
from jax import lax
from jax.sharding import PartitionSpec as P

HIGHEST = lax.Precision.HIGHEST
KV_MODE = "butterfly"


def nesterov(average, state, anchor, outer_rate):
    momentum = 0.5 * state + average
    updated = anchor - outer_rate * (average + 0.5 * momentum)
    return (average, momentum, updated)


def flip(axis, bit):
    n = lax.axis_size(axis)
    return [(i, i ^ (1 << bit)) for i in range(n)]


def all_reduce_doubling(x, steps):
    for axis, bit in steps:
        x = x + lax.ppermute(x, axis, flip(axis, bit))
    return x


def reduce_scatter_halving(x, axis, bits):
    idx = lax.axis_index(axis)
    for bit in bits:
        half = x.shape[0] // 2
        b = (idx >> bit) & 1
        keep = lax.dynamic_slice_in_dim(x, b * half, half)
        send = lax.dynamic_slice_in_dim(x, (1 - b) * half, half)
        x = keep + lax.ppermute(send, axis, flip(axis, bit))
    return x


def all_gather_doubling(x, axis, bits):
    idx = lax.axis_index(axis)
    for bit in bits:
        b = ((idx >> bit) & 1) == 0
        other = lax.ppermute(x, axis, flip(axis, bit))
        x = jnp.concatenate([jnp.where(b, x, other), jnp.where(b, other, x)])
    return x


def local(kv_local, kv_anchor, kv_state, r_local, r_anchor, r_state, g_local, g_anchor, g_state,
          e_local, e_anchor, e_state, basis, rate):
    groups = lax.axis_size("group")
    group_bits = groups.bit_length() - 1
    tensor_bits = lax.axis_size("tensor").bit_length() - 1
    kv_diff = kv_anchor - kv_local[0]
    r_diff = r_anchor - r_local[0]
    g_diff = g_anchor - g_local[0]
    partial = jnp.dot(e_anchor - e_local[0], basis, precision=HIGHEST, preferred_element_type=jnp.float32)
    steps = [("group", b) for b in range(group_bits)] + [("tensor", b) for b in range(tensor_bits)]
    factors = all_reduce_doubling(partial, steps)
    pieces = (kv_diff, r_diff, g_diff)
    flat = jnp.concatenate([p.reshape(-1) for p in pieces])
    if KV_MODE == "butterfly":
        bits = list(range(group_bits))
        total = all_gather_doubling(reduce_scatter_halving(flat, "group", bits), "group", bits[::-1])
    else:
        total = lax.psum(flat, "group")
    sums, at = [], 0
    for p in pieces:
        sums.append(total[at:at + p.size].reshape(p.shape))
        at += p.size
    kv_sum, r_sum, g_sum = sums
    kv_out = nesterov(kv_sum / groups, kv_state, kv_anchor, rate)
    r_out = nesterov(r_sum / groups, r_state, r_anchor, rate)
    g_out = nesterov(g_sum / groups, g_state, g_anchor, rate)
    factors = factors / groups
    e_avg = jnp.dot(factors, basis.T, precision=HIGHEST, preferred_element_type=jnp.float32)
    e_out = nesterov(e_avg, e_state, e_anchor, rate)
    return (*kv_out, *r_out, *g_out, *e_out)


IN_SPECS = (
    P("group", None, "dp", "tensor"), P(None, "dp", "tensor"), P(None, "dp", "tensor"),
    P("group", "dp", None), P("dp", None), P("dp", None),
    P("group", None, "dp"), P(None, "dp"), P(None, "dp"),
    P("group", "dp", "tensor"), P("dp", "tensor"), P("dp", "tensor"),
    P("tensor", None), P(),
)
OUT_SPECS = (
    P(None, "dp", "tensor"), P(None, "dp", "tensor"), P(None, "dp", "tensor"),
    P("dp", None), P("dp", None), P("dp", None),
    P(None, "dp"), P(None, "dp"), P(None, "dp"),
    P("dp", "tensor"), P("dp", "tensor"), P("dp", "tensor"),
)


def solution(mesh):
    return jax.shard_map(local, mesh=mesh, in_specs=IN_SPECS, out_specs=OUT_SPECS, check_vma=False)
```

```python
import jax
import jax.numpy as jnp
from jax import lax
from jax.sharding import PartitionSpec as P

HIGHEST = lax.Precision.HIGHEST
TENSOR_MODE = "a2a"


def nesterov(average, state, anchor, outer_rate):
    momentum = 0.5 * state + average
    updated = anchor - outer_rate * (average + 0.5 * momentum)
    return (average, momentum, updated)


def flip(axis, bit):
    n = lax.axis_size(axis)
    return [(i, i ^ (1 << bit)) for i in range(n)]


def all_reduce_doubling(x, steps):
    for axis, bit in steps:
        x = x + lax.ppermute(x, axis, flip(axis, bit))
    return x


def reduce_scatter_halving(x, axis, bits):
    idx = lax.axis_index(axis)
    for bit in bits:
        half = x.shape[0] // 2
        b = (idx >> bit) & 1
        keep = lax.dynamic_slice_in_dim(x, b * half, half)
        send = lax.dynamic_slice_in_dim(x, (1 - b) * half, half)
        x = keep + lax.ppermute(send, axis, flip(axis, bit))
    return x


def all_gather_doubling(x, axis, bits):
    idx = lax.axis_index(axis)
    for bit in bits:
        b = ((idx >> bit) & 1) == 0
        other = lax.ppermute(x, axis, flip(axis, bit))
        x = jnp.concatenate([jnp.where(b, x, other), jnp.where(b, other, x)])
    return x


def local(kv_local, kv_anchor, kv_state, r_local, r_anchor, r_state, g_local, g_anchor, g_state,
          e_local, e_anchor, e_state, basis, rate):
    groups = lax.axis_size("group")
    group_bits = groups.bit_length() - 1
    tensors = lax.axis_size("tensor")
    tensor_bits = tensors.bit_length() - 1
    kv_diff = kv_anchor - kv_local[0]
    r_diff = r_anchor - r_local[0]
    g_diff = g_anchor - g_local[0]
    partial = jnp.dot(e_anchor - e_local[0], basis, precision=HIGHEST, preferred_element_type=jnp.float32)
    pieces = (kv_diff, r_diff, g_diff, partial)
    flat = jnp.concatenate([p.reshape(-1) for p in pieces])
    bits = list(range(group_bits))
    total = all_gather_doubling(reduce_scatter_halving(flat, "group", bits), "group", bits[::-1])
    sums, at = [], 0
    for p in pieces:
        sums.append(total[at:at + p.size].reshape(p.shape))
        at += p.size
    kv_sum, r_sum, g_sum, factors = sums
    if TENSOR_MODE == "doubling":
        factors = all_reduce_doubling(factors, [("tensor", b) for b in range(tensor_bits)])
    else:
        copies = jnp.broadcast_to(factors[None], (tensors,) + factors.shape)
        factors = jnp.sum(lax.all_to_all(copies, "tensor", 0, 0, tiled=True), axis=0)
    kv_out = nesterov(kv_sum / groups, kv_state, kv_anchor, rate)
    r_out = nesterov(r_sum / groups, r_state, r_anchor, rate)
    g_out = nesterov(g_sum / groups, g_state, g_anchor, rate)
    factors = factors / groups
    e_avg = jnp.dot(factors, basis.T, precision=HIGHEST, preferred_element_type=jnp.float32)
    e_out = nesterov(e_avg, e_state, e_anchor, rate)
    return (*kv_out, *r_out, *g_out, *e_out)


IN_SPECS = (
    P("group", None, "dp", "tensor"), P(None, "dp", "tensor"), P(None, "dp", "tensor"),
    P("group", "dp", None), P("dp", None), P("dp", None),
    P("group", None, "dp"), P(None, "dp"), P(None, "dp"),
    P("group", "dp", "tensor"), P("dp", "tensor"), P("dp", "tensor"),
    P("tensor", None), P(),
)
OUT_SPECS = (
    P(None, "dp", "tensor"), P(None, "dp", "tensor"), P(None, "dp", "tensor"),
    P("dp", None), P("dp", None), P("dp", None),
    P(None, "dp"), P(None, "dp"), P(None, "dp"),
    P("dp", "tensor"), P("dp", "tensor"), P("dp", "tensor"),
)


def solution(mesh):
    return jax.shard_map(local, mesh=mesh, in_specs=IN_SPECS, out_specs=OUT_SPECS, check_vma=False)
```

```python
import jax
import jax.numpy as jnp
from jax import lax
from jax.sharding import PartitionSpec as P

HIGHEST = lax.Precision.HIGHEST


def nesterov(average, state, anchor, outer_rate):
    momentum = 0.5 * state + average
    updated = anchor - outer_rate * (average + 0.5 * momentum)
    return (average, momentum, updated)


def flip(axis, bit):
    n = lax.axis_size(axis)
    return [(i, i ^ (1 << bit)) for i in range(n)]


def all_reduce_doubling(x, steps):
    for axis, bit in steps:
        x = x + lax.ppermute(x, axis, flip(axis, bit))
    return x


def reduce_scatter_halving(x, axis, bits):
    idx = lax.axis_index(axis)
    for bit in bits:
        half = x.shape[0] // 2
        b = (idx >> bit) & 1
        keep = lax.dynamic_slice_in_dim(x, b * half, half)
        send = lax.dynamic_slice_in_dim(x, (1 - b) * half, half)
        x = keep + lax.ppermute(send, axis, flip(axis, bit))
    return x


def all_gather_doubling(x, axis, bits):
    idx = lax.axis_index(axis)
    for bit in bits:
        b = ((idx >> bit) & 1) == 0
        other = lax.ppermute(x, axis, flip(axis, bit))
        x = jnp.concatenate([jnp.where(b, x, other), jnp.where(b, other, x)])
    return x


def local(kv_local, kv_anchor, kv_state, r_local, r_anchor, r_state, g_local, g_anchor, g_state,
          e_local, e_anchor, e_state, basis, rate):
    groups = lax.axis_size("group")
    group_bits = groups.bit_length() - 1
    tensor_bits = lax.axis_size("tensor").bit_length() - 1
    kv_diff = kv_anchor - kv_local[0]
    r_diff = r_anchor - r_local[0]
    g_diff = g_anchor - g_local[0]
    partial = jnp.dot(e_anchor - e_local[0], basis, precision=HIGHEST, preferred_element_type=jnp.float32)
    tile = 1024
    f = partial.reshape(-1)
    f = jnp.pad(f, (0, -f.shape[0] % tile))
    width = f.shape[0]
    pieces = (kv_diff, r_diff, g_diff)
    x = jnp.concatenate([p.reshape(-1) for p in pieces])
    x = jnp.pad(x, (0, -x.shape[0] % (groups * tile)))
    gidx = lax.axis_index("group")
    bits = list(range(group_bits))
    for bit in bits:
        half = x.shape[0] // 2
        b = (gidx >> bit) & 1
        keep = lax.dynamic_slice_in_dim(x, b * half, half)
        send = lax.dynamic_slice_in_dim(x, (1 - b) * half, half)
        got = lax.ppermute(jnp.concatenate([f, send]), "group", flip("group", bit))
        f = f + got[:width]
        x = keep + got[width:]
    tensor_steps = list(range(tensor_bits))
    for bit in bits[::-1]:
        low = ((gidx >> bit) & 1) == 0
        other = lax.ppermute(x, "group", flip("group", bit))
        if tensor_steps:
            t = tensor_steps.pop(0)
            f = f + lax.ppermute(f, "tensor", flip("tensor", t))
        x = jnp.concatenate([jnp.where(low, x, other), jnp.where(low, other, x)])
    for t in tensor_steps:
        f = f + lax.ppermute(f, "tensor", flip("tensor", t))
    total = x
    sums, at = [], 0
    for p in pieces:
        sums.append(total[at:at + p.size].reshape(p.shape))
        at += p.size
    kv_sum, r_sum, g_sum = sums
    kv_out = nesterov(kv_sum / groups, kv_state, kv_anchor, rate)
    r_out = nesterov(r_sum / groups, r_state, r_anchor, rate)
    g_out = nesterov(g_sum / groups, g_state, g_anchor, rate)
    factors = f[:partial.size].reshape(partial.shape) / groups
    e_avg = jnp.dot(factors, basis.T, precision=HIGHEST, preferred_element_type=jnp.float32)
    e_out = nesterov(e_avg, e_state, e_anchor, rate)
    return (*kv_out, *r_out, *g_out, *e_out)


IN_SPECS = (
    P("group", None, "dp", "tensor"), P(None, "dp", "tensor"), P(None, "dp", "tensor"),
    P("group", "dp", None), P("dp", None), P("dp", None),
    P("group", None, "dp"), P(None, "dp"), P(None, "dp"),
    P("group", "dp", "tensor"), P("dp", "tensor"), P("dp", "tensor"),
    P("tensor", None), P(),
)
OUT_SPECS = (
    P(None, "dp", "tensor"), P(None, "dp", "tensor"), P(None, "dp", "tensor"),
    P("dp", None), P("dp", None), P("dp", None),
    P(None, "dp"), P(None, "dp"), P(None, "dp"),
    P("dp", "tensor"), P("dp", "tensor"), P("dp", "tensor"),
)


def solution(mesh):
    return jax.shard_map(local, mesh=mesh, in_specs=IN_SPECS, out_specs=OUT_SPECS, check_vma=False)
```

```python
import jax
import jax.numpy as jnp
from jax import lax
from jax.sharding import PartitionSpec as P

HIGHEST = lax.Precision.HIGHEST


def nesterov(average, state, anchor, outer_rate):
    momentum = 0.5 * state + average
    updated = anchor - outer_rate * (average + 0.5 * momentum)
    return (average, momentum, updated)


def flip(axis, bit):
    n = lax.axis_size(axis)
    return [(i, i ^ (1 << bit)) for i in range(n)]


def all_reduce_doubling(x, steps):
    for axis, bit in steps:
        x = x + lax.ppermute(x, axis, flip(axis, bit))
    return x


def reduce_scatter_halving(x, axis, bits):
    idx = lax.axis_index(axis)
    for bit in bits:
        half = x.shape[0] // 2
        b = (idx >> bit) & 1
        keep = lax.dynamic_slice_in_dim(x, b * half, half)
        send = lax.dynamic_slice_in_dim(x, (1 - b) * half, half)
        x = keep + lax.ppermute(send, axis, flip(axis, bit))
    return x


def all_gather_doubling(x, axis, bits):
    idx = lax.axis_index(axis)
    for bit in bits:
        b = ((idx >> bit) & 1) == 0
        other = lax.ppermute(x, axis, flip(axis, bit))
        x = jnp.concatenate([jnp.where(b, x, other), jnp.where(b, other, x)])
    return x


def local(kv_local, kv_anchor, kv_state, r_local, r_anchor, r_state, g_local, g_anchor, g_state,
          e_local, e_anchor, e_state, basis, rate):
    groups = lax.axis_size("group")
    group_bits = groups.bit_length() - 1
    tensor_bits = lax.axis_size("tensor").bit_length() - 1
    kv_diff = kv_anchor - kv_local[0]
    r_diff = r_anchor - r_local[0]
    g_diff = g_anchor - g_local[0]
    partial = jnp.dot(e_anchor - e_local[0], basis, precision=HIGHEST, preferred_element_type=jnp.float32)
    tile = 1024
    f = partial.reshape(-1)
    f = jnp.pad(f, (0, -f.shape[0] % tile))
    width = f.shape[0]
    pieces = (kv_diff, r_diff, g_diff)
    x = jnp.concatenate([p.reshape(-1) for p in pieces])
    x = jnp.pad(x, (0, -x.shape[0] % (groups * tile)))
    gidx = lax.axis_index("group")
    bits = list(range(group_bits))
    for bit in bits:
        half = x.shape[0] // 2
        b = (gidx >> bit) & 1
        keep = lax.dynamic_slice_in_dim(x, b * half, half)
        send = lax.dynamic_slice_in_dim(x, (1 - b) * half, half)
        got = lax.ppermute(jnp.concatenate([f, send]), "group", flip("group", bit))
        f = f + got[:width]
        x = keep + got[width:]
    tensor_steps = list(range(tensor_bits))[::-1]
    for bit in bits[::-1]:
        low = ((gidx >> bit) & 1) == 0
        other = lax.ppermute(x, "group", flip("group", bit))
        if tensor_steps:
            t = tensor_steps.pop(0)
            f = f + lax.ppermute(f, "tensor", flip("tensor", t))
        x = jnp.concatenate([jnp.where(low, x, other), jnp.where(low, other, x)])
    for t in tensor_steps:
        f = f + lax.ppermute(f, "tensor", flip("tensor", t))
    total = x
    sums, at = [], 0
    for p in pieces:
        sums.append(total[at:at + p.size].reshape(p.shape))
        at += p.size
    kv_sum, r_sum, g_sum = sums
    kv_out = nesterov(kv_sum / groups, kv_state, kv_anchor, rate)
    r_out = nesterov(r_sum / groups, r_state, r_anchor, rate)
    g_out = nesterov(g_sum / groups, g_state, g_anchor, rate)
    factors = f[:partial.size].reshape(partial.shape) / groups
    e_avg = jnp.dot(factors, basis.T, precision=HIGHEST, preferred_element_type=jnp.float32)
    e_out = nesterov(e_avg, e_state, e_anchor, rate)
    return (*kv_out, *r_out, *g_out, *e_out)


IN_SPECS = (
    P("group", None, "dp", "tensor"), P(None, "dp", "tensor"), P(None, "dp", "tensor"),
    P("group", "dp", None), P("dp", None), P("dp", None),
    P("group", None, "dp"), P(None, "dp"), P(None, "dp"),
    P("group", "dp", "tensor"), P("dp", "tensor"), P("dp", "tensor"),
    P("tensor", None), P(),
)
OUT_SPECS = (
    P(None, "dp", "tensor"), P(None, "dp", "tensor"), P(None, "dp", "tensor"),
    P("dp", None), P("dp", None), P("dp", None),
    P(None, "dp"), P(None, "dp"), P(None, "dp"),
    P("dp", "tensor"), P("dp", "tensor"), P("dp", "tensor"),
)


def solution(mesh):
    return jax.shard_map(local, mesh=mesh, in_specs=IN_SPECS, out_specs=OUT_SPECS, check_vma=False)
```
